128 devices in a mesh: req: 32 (over z, x, core), tok: 4 (over y).
Axes of the slice: x: 4, y: 4, z: 4, core: 2. Of those that a mesh axis runs over, the one named last changes fastest.
Arguments:
- tokens: bfloat16 [32768, 1280], P(('req', 'tok')), may hold values from -6 to 6
- segments: int32 [32, 1024], P('req'), may hold values from 0 to 16, as said below
- gain_attn: float32 [1280], replicated, may hold values from 0.1 to 1.9
- w_qkv: bfloat16 [1280, 3, 1280], P(None, None, 'tok'), may hold values from -1 to 1
- w_out: bfloat16 [1280, 1280], P('tok'), may hold values from -0.15625 to 0.15625
- gain_mlp: float32 [1280], replicated, may hold values from 0.1 to 1.9
- w_up: bfloat16 [1280, 5120], P(None, ('req', 'tok')), may hold values from -0.15625 to 0.15625
- w_down_t: bfloat16 [1280, 5120], P(None, ('req', 'tok')), may hold values from -0.078125 to 0.078125
- gain_merge: float32 [1280], replicated, may hold values from 0.1 to 1.9
- w_proj: bfloat16 [5120, 4096], P(None, 'tok'), may hold values from -0.078125 to 0.078125
Outputs:
- owned: bfloat16 [8192, 4096], P('req', 'tok')
The draws below stay inside these ranges and needn't reach their ends.
Inputs may be any that keep to these rules, and one draw needn't show every extreme that they name: `segments`: in each row segment ids start at 0 and never fall; every image covers whole aligned runs of 4 positions and at most 512 positions; image 0 of every row covers exactly 512, and every row holds exactly max(1, 16) + 1 images.
All inputs are finite; a program needn't handle non-finite values.
Results may differ from the reference program's by a relative error of at most 0.015.
The reference program's roundings to bfloat16 on the way count: a program that leaves them out, or rounds other values in their place, can miss the bound.
Values may be sent and summed in bfloat16 or wider, within the bound.
No kernel may reach another device: no remote copies, remote signals or barrier semaphores. Data moves between devices by JAX's collectives and lax.ppermute only.
A program may use at most 128 MiB of HBM per device.

```python
import math
import jax
import jax.numpy as jnp
from jax import lax

HEADS = 16
HDIM = 80
FF = 5120
OUT = 4096
D = 1280
GROUP = 1024
MOST_IMG = 512
TOKENS = 32768
ROWS = 8192
BU = 8
N_REQ = 32


def draw_segments(key, part):
    units = GROUP // 4
    most = MOST_IMG // 4
    rest = units - most
    extra = max(1, GROUP // 64)
    row_keys = jax.random.split(key, N_REQ)
    orders = jax.vmap(lambda row_key: jax.random.permutation(row_key, rest - 1))(row_keys)
    chosen = (orders[:, :extra - 1] + most + 1).astype(jnp.int32)
    position = jnp.arange(units, dtype=jnp.int32)
    picked = jnp.any(position[None, None, :] == chosen[:, :, None], axis=1)
    starts = jnp.logical_or(picked, (position == most)[None, :]).astype(jnp.int32)
    unit_ids = jnp.cumsum(starts, axis=1).astype(jnp.int32)
    return jnp.repeat(unit_ids, 4, axis=1).astype(jnp.int32)


def draw_w_qkv(key, part):
    noise_key = jax.random.fold_in(key, 0)
    width = HEADS * HDIM
    weights = jax.random.truncated_normal(noise_key, -6.0, 6.0, (width, 3, width), jnp.float32) * width ** (-0.5)
    return jnp.clip(weights, -1.0, 1.0).astype(jnp.bfloat16)


def levels(own_key, dims, shards, smallest, top_value):
    level, own = 1.0, jax.random.fold_in(own_key, 6)
    for axis_at, blocks in shards:
        steps = jnp.exp(jax.random.uniform(jax.random.fold_in(own, axis_at), (blocks,), jnp.float32, smallest / len(shards), top_value / len(shards)))
        level = level * jnp.repeat(steps, dims[axis_at] // blocks).reshape([-1 if axis == axis_at else 1 for axis in range(len(dims))])
    return level


def gaussian(key, extent, scale, limit, cuts=(), held_as=jnp.bfloat16):
    values = jax.random.normal(key, extent, jnp.float32) * scale
    if len(cuts) > 0:
        values = levels(key, extent, cuts, -0.22, 0.18) * values
    return jnp.clip(values, min=-limit, max=limit).astype(held_as)


def setup_inputs(seed: int = 0) -> dict:
    splits = jax.random.split(jax.random.key(seed), 11)
    tokens = gaussian(splits[0], (TOKENS, D), 1.0, 6.0, ((0, 128),))
    segments = draw_segments(jax.random.fold_in(splits[10], 71), 0)
    gain_attn = jnp.clip(1.0 + 0.18 * jax.random.normal(splits[2], (D,), jnp.float32), 0.1, 1.9)
    w_qkv = draw_w_qkv(jax.random.fold_in(splits[10], 71), 0)
    w_out = gaussian(splits[4], (D, D), D ** -0.5, 0.15625, ((0, 4),))
    gain_mlp = jnp.clip(1.0 + 0.18 * jax.random.normal(splits[5], (D,), jnp.float32), 0.1, 1.9)
    w_up = gaussian(splits[6], (D, FF), D ** -0.5, 0.15625, ((1, 128),))
    w_down_t = gaussian(splits[7], (D, FF), FF ** -0.5, 0.078125, ((1, 128),))
    gain_merge = jnp.clip(1.0 + 0.18 * jax.random.normal(splits[8], (D,), jnp.float32), 0.1, 1.9)
    w_proj = gaussian(splits[9], (4 * D, OUT), (4 * D) ** -0.5, 0.078125, ((1, 4),))
    return {"tokens": tokens, "segments": segments, "gain_attn": gain_attn, "w_qkv": w_qkv, "w_out": w_out, "gain_mlp": gain_mlp, "w_up": w_up, "w_down_t": w_down_t, "gain_merge": gain_merge, "w_proj": w_proj}


def layer_norm(values, gain):
    mean = lax.optimization_barrier(jnp.mean(values, axis=-1, keepdims=True))
    centered = values - mean
    spread = lax.optimization_barrier(jnp.mean(centered * centered, axis=-1, keepdims=True))
    return centered * lax.rsqrt(spread + 1e-06) * gain

def reference(tokens, segments, gain_attn, w_qkv, w_out, gain_mlp, w_up, w_down_t, gain_merge, w_proj):
    width = HEADS * HDIM
    inputs = tokens.astype(jnp.float32)
    normed = layer_norm(inputs, gain_attn).astype(jnp.bfloat16)
    queries = jnp.dot(normed, w_qkv[:, 0, :], preferred_element_type=jnp.float32).astype(jnp.bfloat16)
    keys_all = jnp.dot(normed, w_qkv[:, 1, :], preferred_element_type=jnp.float32).astype(jnp.bfloat16)
    values_all = jnp.dot(normed, w_qkv[:, 2, :], preferred_element_type=jnp.float32).astype(jnp.bfloat16)
    scale = 1.0 / math.sqrt(HDIM)

    def one_group(packed):
        query_rows, key_rows, value_rows, images = packed
        query_f = query_rows.astype(jnp.float32).reshape(GROUP, HEADS, HDIM)
        key_f = key_rows.astype(jnp.float32).reshape(GROUP, HEADS, HDIM)
        value_f = value_rows.astype(jnp.float32).reshape(GROUP, HEADS, HDIM)
        scores = jnp.einsum('qhd,khd->hqk', query_f, key_f) * scale
        same = images[:, None] == images[None, :]
        scores = jnp.where(same[None], scores, -1e+30)
        row_max = lax.optimization_barrier(jnp.max(scores, axis=-1, keepdims=True))
        expo = jnp.exp(scores - row_max)
        weights = (expo / lax.optimization_barrier(jnp.sum(expo, axis=-1, keepdims=True))).astype(jnp.bfloat16)
        mixed = jnp.einsum('hqk,khd->qhd', weights.astype(jnp.float32), value_f)
        return mixed.reshape(GROUP, width).astype(jnp.bfloat16)
    grouped = lax.map(one_group, (queries.reshape(N_REQ, GROUP, width), keys_all.reshape(N_REQ, GROUP, width), values_all.reshape(N_REQ, GROUP, width), segments))
    heads_out = grouped.reshape(TOKENS, width)
    attended = jnp.dot(heads_out, w_out, preferred_element_type=jnp.float32)
    first = (inputs + attended).astype(jnp.bfloat16)
    normed_mlp = layer_norm(first.astype(jnp.float32), gain_mlp).astype(jnp.bfloat16)
    hidden = jax.nn.gelu(jnp.dot(normed_mlp, w_up, preferred_element_type=jnp.float32), approximate=False).astype(jnp.bfloat16)
    mlp_out = jnp.dot(hidden, w_down_t.T, preferred_element_type=jnp.float32)
    second = first.astype(jnp.float32) + mlp_out
    normed_merge = layer_norm(second, gain_merge).astype(jnp.bfloat16)
    merged = normed_merge.reshape(TOKENS // 4, 4 * width)
    projected = jnp.dot(merged, w_proj, preferred_element_type=jnp.float32).astype(jnp.bfloat16)
    owned = projected.reshape(N_REQ, N_REQ, BU, OUT).transpose(1, 0, 2, 3).reshape(ROWS, OUT)
    return owned
```

```python
import math

import jax
import jax.numpy as jnp
from jax import lax
from jax.sharding import Mesh, PartitionSpec as P


HDIM = 80


def layer_norm(values, gain):
    mean = jnp.mean(values, axis=-1, keepdims=True)
    centered = values - mean
    spread = jnp.mean(centered * centered, axis=-1, keepdims=True)
    return centered * lax.rsqrt(spread + 1e-06) * gain


def hidden_fold(rows, pieces):
    up_piece, down_piece = pieces
    hidden = jax.nn.gelu(
        jnp.dot(rows, up_piece, preferred_element_type=jnp.float32), approximate=False
    ).astype(jnp.bfloat16)
    return lax.dot_general(
        hidden, down_piece, (((1,), (1,)), ((), ())), preferred_element_type=jnp.float32
    )


def attend_block(
    queries,
    keys_blocked,
    values_blocked,
    images,
    images_blocked,
    first_row,
    q_block,
    k_block,
    scale,
):
    local_heads = keys_blocked.shape[2]
    query_part = queries[first_row : first_row + q_block].reshape(q_block, local_heads, HDIM)
    query_images = images[first_row : first_row + q_block]
    key_first = jnp.sum((images < images[first_row]).astype(jnp.int32))
    key_last = jnp.sum((images <= images[first_row + q_block - 1]).astype(jnp.int32))
    block_first = key_first // k_block
    block_last = (key_last + k_block - 1) // k_block

    def block_scores(kblock):
        scores = (
            jnp.einsum(
                "qhd,khd->hqk", query_part, keys_blocked[kblock], preferred_element_type=jnp.float32
            )
            * scale
        )
        same = query_images[:, None] == images_blocked[kblock][None, :]
        return jnp.where(same[None], scores, -1e30)

    def scan_stats(kblock, carry):
        row_max, row_sum = carry
        scores = block_scores(kblock)
        new_max = jnp.maximum(row_max, jnp.max(scores, axis=-1))
        row_sum = row_sum * jnp.exp(row_max - new_max) + jnp.sum(
            jnp.exp(scores - new_max[..., None]), axis=-1
        )
        return (new_max, row_sum)

    start_max = jnp.full((local_heads, q_block), -1e30, jnp.float32)
    start_sum = jnp.zeros((local_heads, q_block), jnp.float32)
    row_max, row_sum = lax.fori_loop(block_first, block_last, scan_stats, (start_max, start_sum))

    def add_values(kblock, totals):
        scores = block_scores(kblock)
        weights = (jnp.exp(scores - row_max[..., None]) / row_sum[..., None]).astype(jnp.bfloat16)
        return totals + jnp.einsum(
            "hqk,khd->qhd", weights, values_blocked[kblock], preferred_element_type=jnp.float32
        )

    totals = lax.fori_loop(
        block_first, block_last, add_values, jnp.zeros((q_block, local_heads, HDIM), jnp.float32)
    )
    return totals.reshape(q_block, local_heads * HDIM).astype(jnp.bfloat16)


def layer(tokens, segments, gain_attn, w_qkv, w_out, gain_mlp, w_up, w_down_t, gain_merge, w_proj):
    up_full = lax.all_gather(w_up, ("zx", "tok"), axis=1, tiled=True)
    down_full = lax.all_gather(w_down_t, ("zx", "tok"), axis=1, tiled=True)
    inputs = tokens.astype(jnp.float32)
    normed = layer_norm(inputs, gain_attn).astype(jnp.bfloat16)
    local_width = w_qkv.shape[2]
    joined = w_qkv.reshape(w_qkv.shape[0], 3 * local_width)
    stacked = jnp.dot(
        lax.all_gather(normed, "tok", axis=0, tiled=True),
        joined,
        preferred_element_type=jnp.float32,
    ).astype(jnp.bfloat16)
    group = stacked.shape[0]
    local_heads = local_width // HDIM
    q_block = min(512, group)
    k_block = min(128, group)
    scale = 1.0 / math.sqrt(HDIM)
    queries = stacked[:, :local_width]
    keys_blocked = stacked[:, local_width : 2 * local_width].reshape(
        group // k_block, k_block, local_heads, HDIM
    )
    values_blocked = stacked[:, 2 * local_width :].reshape(
        group // k_block, k_block, local_heads, HDIM
    )
    images = segments[0]
    images_blocked = images.reshape(group // k_block, k_block)
    outputs = []
    for block in range(group // q_block):
        outputs.append(
            attend_block(
                queries,
                keys_blocked,
                values_blocked,
                images,
                images_blocked,
                block * q_block,
                q_block,
                k_block,
                scale,
            )
        )
    heads_out = jnp.concatenate(outputs, axis=0)
    attended = lax.psum_scatter(
        jnp.dot(heads_out, w_out, preferred_element_type=jnp.float32).astype(jnp.bfloat16),
        "tok",
        scatter_dimension=0,
        tiled=True,
    ).astype(jnp.float32)
    first = (inputs + attended).astype(jnp.bfloat16)
    normed_mlp = layer_norm(first.astype(jnp.float32), gain_mlp).astype(jnp.bfloat16)
    mlp_out = lax.psum_scatter(
        hidden_fold(
            lax.all_gather(normed_mlp, "core", axis=0, tiled=True),
            (up_full, down_full),
        ),
        "core",
        scatter_dimension=0,
        tiled=True,
    )
    second = first.astype(jnp.float32) + mlp_out
    normed_merge = layer_norm(second, gain_merge).astype(jnp.bfloat16)
    merged = normed_merge.reshape(inputs.shape[0] // 4, 4 * inputs.shape[1])
    projected = jnp.dot(
        lax.all_gather(merged, "tok", axis=0, tiled=True),
        w_proj,
        preferred_element_type=jnp.float32,
    ).astype(jnp.bfloat16)
    return lax.all_to_all(projected, ("zx", "core"), split_axis=0, concat_axis=0, tiled=True)


def solution(mesh):
    devices = mesh.devices
    split = Mesh(devices.reshape(devices.shape[0] // 2, 2, devices.shape[1]), ("zx", "core", "tok"))
    rows = ("zx", "core")
    return jax.shard_map(
        layer,
        mesh=split,
        in_specs=(
            P(rows + ("tok",), None),
            P(rows, None),
            P(),
            P(None, None, "tok"),
            P("tok", None),
            P(),
            P(None, rows + ("tok",)),
            P(None, rows + ("tok",)),
            P(),
            P(None, "tok"),
        ),
        out_specs=P(rows, "tok"),
        check_vma=False,
    )
```

```python
import math

import jax
import jax.numpy as jnp
from jax import lax
from jax.sharding import Mesh, PartitionSpec as P


HDIM = 80


def layer_norm(values, gain):
    mean = jnp.mean(values, axis=-1, keepdims=True)
    centered = values - mean
    spread = jnp.mean(centered * centered, axis=-1, keepdims=True)
    return centered * lax.rsqrt(spread + 1e-06) * gain


def attend_block(
    queries,
    keys_blocked,
    values_blocked,
    images,
    images_blocked,
    first_row,
    q_block,
    k_block,
    scale,
):
    local_heads = keys_blocked.shape[2]
    query_part = queries[first_row : first_row + q_block].reshape(q_block, local_heads, HDIM)
    query_images = images[first_row : first_row + q_block]
    key_first = jnp.sum((images < images[first_row]).astype(jnp.int32))
    key_last = jnp.sum((images <= images[first_row + q_block - 1]).astype(jnp.int32))
    block_first = key_first // k_block
    block_last = (key_last + k_block - 1) // k_block

    def block_scores(kblock):
        scores = (
            jnp.einsum(
                "qhd,khd->hqk", query_part, keys_blocked[kblock], preferred_element_type=jnp.float32
            )
            * scale
        )
        same = query_images[:, None] == images_blocked[kblock][None, :]
        return jnp.where(same[None], scores, -1e30)

    def scan_stats(kblock, carry):
        row_max, row_sum = carry
        scores = block_scores(kblock)
        new_max = jnp.maximum(row_max, jnp.max(scores, axis=-1))
        row_sum = row_sum * jnp.exp(row_max - new_max) + jnp.sum(
            jnp.exp(scores - new_max[..., None]), axis=-1
        )
        return (new_max, row_sum)

    start_max = jnp.full((local_heads, q_block), -1e30, jnp.float32)
    start_sum = jnp.zeros((local_heads, q_block), jnp.float32)
    row_max, row_sum = lax.fori_loop(block_first, block_last, scan_stats, (start_max, start_sum))

    def add_values(kblock, totals):
        scores = block_scores(kblock)
        weights = (jnp.exp(scores - row_max[..., None]) / row_sum[..., None]).astype(jnp.bfloat16)
        return totals + jnp.einsum(
            "hqk,khd->qhd", weights, values_blocked[kblock], preferred_element_type=jnp.float32
        )

    totals = lax.fori_loop(
        block_first, block_last, add_values, jnp.zeros((q_block, local_heads, HDIM), jnp.float32)
    )
    return totals.reshape(q_block, local_heads * HDIM).astype(jnp.bfloat16)


def layer(tokens, segments, gain_attn, w_qkv, w_out, gain_mlp, w_up, w_down_t, gain_merge, w_proj):
    every = ("zx", "core", "tok")
    up_full = lax.all_gather(w_up, every, axis=1, tiled=True)
    piece = w_down_t.shape[0] // CHUNKS
    down_parts = []
    for chunk in range(CHUNKS):
        down_parts.append(
            lax.all_gather(w_down_t[chunk * piece : (chunk + 1) * piece], every, axis=1, tiled=True)
        )
    inputs = tokens.astype(jnp.float32)
    normed = layer_norm(inputs, gain_attn).astype(jnp.bfloat16)
    local_width = w_qkv.shape[2]
    joined = w_qkv.reshape(w_qkv.shape[0], 3 * local_width)
    stacked = jnp.dot(
        lax.all_gather(normed, "tok", axis=0, tiled=True),
        joined,
        preferred_element_type=jnp.float32,
    ).astype(jnp.bfloat16)
    group = stacked.shape[0]
    local_heads = local_width // HDIM
    q_block = min(512, group)
    k_block = min(128, group)
    scale = 1.0 / math.sqrt(HDIM)
    queries = stacked[:, :local_width]
    keys_blocked = stacked[:, local_width : 2 * local_width].reshape(
        group // k_block, k_block, local_heads, HDIM
    )
    values_blocked = stacked[:, 2 * local_width :].reshape(
        group // k_block, k_block, local_heads, HDIM
    )
    images = segments[0]
    images_blocked = images.reshape(group // k_block, k_block)
    outputs = []
    for block in range(group // q_block):
        outputs.append(
            attend_block(
                queries,
                keys_blocked,
                values_blocked,
                images,
                images_blocked,
                block * q_block,
                q_block,
                k_block,
                scale,
            )
        )
    heads_out = jnp.concatenate(outputs, axis=0)
    attended = lax.psum_scatter(
        jnp.dot(heads_out, w_out, preferred_element_type=jnp.float32).astype(jnp.bfloat16),
        "tok",
        scatter_dimension=0,
        tiled=True,
    ).astype(jnp.float32)
    first = (inputs + attended).astype(jnp.bfloat16)
    normed_mlp = layer_norm(first.astype(jnp.float32), gain_mlp).astype(jnp.bfloat16)
    hidden = jax.nn.gelu(
        jnp.dot(normed_mlp, up_full, preferred_element_type=jnp.float32), approximate=False
    ).astype(jnp.bfloat16)
    hidden = lax.optimization_barrier(hidden)
    first_f = first.astype(jnp.float32)
    pieces = []
    for chunk in range(CHUNKS):
        pieces.append(
            lax.optimization_barrier(
                first_f[:, chunk * piece : (chunk + 1) * piece]
                + lax.dot_general(
                    hidden,
                    down_parts[chunk],
                    (((1,), (1,)), ((), ())),
                    preferred_element_type=jnp.float32,
                )
            )
        )
    second = jnp.concatenate(pieces, axis=1)
    normed_merge = layer_norm(second, gain_merge).astype(jnp.bfloat16)
    merged = normed_merge.reshape(inputs.shape[0] // 4, 4 * inputs.shape[1])
    projected = jnp.dot(
        lax.all_gather(merged, "tok", axis=0, tiled=True),
        w_proj,
        preferred_element_type=jnp.float32,
    ).astype(jnp.bfloat16)
    return lax.all_to_all(projected, ("zx", "core"), split_axis=0, concat_axis=0, tiled=True)


CHUNKS = 4


def solution(mesh):
    devices = mesh.devices
    split = Mesh(devices.reshape(devices.shape[0] // 2, 2, devices.shape[1]), ("zx", "core", "tok"))
    rows = ("zx", "core")
    return jax.shard_map(
        layer,
        mesh=split,
        in_specs=(
            P(rows + ("tok",), None),
            P(rows, None),
            P(),
            P(None, None, "tok"),
            P("tok", None),
            P(),
            P(None, rows + ("tok",)),
            P(None, rows + ("tok",)),
            P(),
            P(None, "tok"),
        ),
        out_specs=P(rows, "tok"),
        check_vma=False,
    )
```

```python
import math

import jax
import jax.numpy as jnp
from jax import lax
from jax.sharding import Mesh, PartitionSpec as P


HDIM = 80


def layer_norm(values, gain):
    mean = jnp.mean(values, axis=-1, keepdims=True)
    centered = values - mean
    spread = jnp.mean(centered * centered, axis=-1, keepdims=True)
    return centered * lax.rsqrt(spread + 1e-06) * gain


def hidden_fold(rows, pieces):
    up_piece, down_piece = pieces
    hidden = jax.nn.gelu(
        jnp.dot(rows, up_piece, preferred_element_type=jnp.float32), approximate=False
    ).astype(jnp.bfloat16)
    return lax.dot_general(
        hidden, down_piece, (((1,), (1,)), ((), ())), preferred_element_type=jnp.float32
    )


def attend_block(
    queries,
    keys_blocked,
    values_blocked,
    images,
    images_blocked,
    first_row,
    q_block,
    k_block,
    scale,
):
    local_heads = keys_blocked.shape[2]
    query_part = queries[first_row : first_row + q_block].reshape(q_block, local_heads, HDIM)
    query_images = images[first_row : first_row + q_block]
    key_first = jnp.sum((images < images[first_row]).astype(jnp.int32))
    key_last = jnp.sum((images <= images[first_row + q_block - 1]).astype(jnp.int32))
    block_first = key_first // k_block
    block_last = (key_last + k_block - 1) // k_block

    def block_scores(kblock):
        scores = (
            jnp.einsum(
                "qhd,khd->hqk", query_part, keys_blocked[kblock], preferred_element_type=jnp.float32
            )
            * scale
        )
        same = query_images[:, None] == images_blocked[kblock][None, :]
        return jnp.where(same[None], scores, -1e30)

    def scan_stats(kblock, carry):
        row_max, row_sum = carry
        scores = block_scores(kblock)
        new_max = jnp.maximum(row_max, jnp.max(scores, axis=-1))
        row_sum = row_sum * jnp.exp(row_max - new_max) + jnp.sum(
            jnp.exp(scores - new_max[..., None]), axis=-1
        )
        return (new_max, row_sum)

    start_max = jnp.full((local_heads, q_block), -1e30, jnp.float32)
    start_sum = jnp.zeros((local_heads, q_block), jnp.float32)
    row_max, row_sum = lax.fori_loop(block_first, block_last, scan_stats, (start_max, start_sum))

    def add_values(kblock, totals):
        scores = block_scores(kblock)
        weights = (jnp.exp(scores - row_max[..., None]) / row_sum[..., None]).astype(jnp.bfloat16)
        return totals + jnp.einsum(
            "hqk,khd->qhd", weights, values_blocked[kblock], preferred_element_type=jnp.float32
        )

    totals = lax.fori_loop(
        block_first, block_last, add_values, jnp.zeros((q_block, local_heads, HDIM), jnp.float32)
    )
    return totals.reshape(q_block, local_heads * HDIM).astype(jnp.bfloat16)


def layer(tokens, segments, gain_attn, w_qkv, w_out, gain_mlp, w_up, w_down_t, gain_merge, w_proj):
    both = lax.all_gather(jnp.stack([w_up, w_down_t]), ("zx", "core", "tok"), axis=2, tiled=True)
    up_full, down_full = both[0], both[1]
    inputs = tokens.astype(jnp.float32)
    normed = layer_norm(inputs, gain_attn).astype(jnp.bfloat16)
    local_width = w_qkv.shape[2]
    joined = w_qkv.reshape(w_qkv.shape[0], 3 * local_width)
    stacked = jnp.dot(
        lax.all_gather(normed, "tok", axis=0, tiled=True),
        joined,
        preferred_element_type=jnp.float32,
    ).astype(jnp.bfloat16)
    group = stacked.shape[0]
    local_heads = local_width // HDIM
    q_block = min(512, group)
    k_block = min(128, group)
    scale = 1.0 / math.sqrt(HDIM)
    queries = stacked[:, :local_width]
    keys_blocked = stacked[:, local_width : 2 * local_width].reshape(
        group // k_block, k_block, local_heads, HDIM
    )
    values_blocked = stacked[:, 2 * local_width :].reshape(
        group // k_block, k_block, local_heads, HDIM
    )
    images = segments[0]
    images_blocked = images.reshape(group // k_block, k_block)
    outputs = []
    for block in range(group // q_block):
        outputs.append(
            attend_block(
                queries,
                keys_blocked,
                values_blocked,
                images,
                images_blocked,
                block * q_block,
                q_block,
                k_block,
                scale,
            )
        )
    heads_out = jnp.concatenate(outputs, axis=0)
    attended = lax.psum_scatter(
        jnp.dot(heads_out, w_out, preferred_element_type=jnp.float32).astype(jnp.bfloat16),
        "tok",
        scatter_dimension=0,
        tiled=True,
    ).astype(jnp.float32)
    first = (inputs + attended).astype(jnp.bfloat16)
    normed_mlp = layer_norm(first.astype(jnp.float32), gain_mlp).astype(jnp.bfloat16)
    mlp_out = hidden_fold(normed_mlp, (up_full, down_full))
    second = first.astype(jnp.float32) + mlp_out
    normed_merge = layer_norm(second, gain_merge).astype(jnp.bfloat16)
    merged = normed_merge.reshape(inputs.shape[0] // 4, 4 * inputs.shape[1])
    projected = jnp.dot(
        lax.all_gather(merged, "tok", axis=0, tiled=True),
        w_proj,
        preferred_element_type=jnp.float32,
    ).astype(jnp.bfloat16)
    return lax.all_to_all(projected, ("zx", "core"), split_axis=0, concat_axis=0, tiled=True)


def solution(mesh):
    devices = mesh.devices
    split = Mesh(devices.reshape(devices.shape[0] // 2, 2, devices.shape[1]), ("zx", "core", "tok"))
    rows = ("zx", "core")
    return jax.shard_map(
        layer,
        mesh=split,
        in_specs=(
            P(rows + ("tok",), None),
            P(rows, None),
            P(),
            P(None, None, "tok"),
            P("tok", None),
            P(),
            P(None, rows + ("tok",)),
            P(None, rows + ("tok",)),
            P(),
            P(None, "tok"),
        ),
        out_specs=P(rows, "tok"),
        check_vma=False,
    )
```

```python
import math

import jax
import jax.numpy as jnp
from jax import lax
from jax.sharding import Mesh, PartitionSpec as P


HDIM = 80


def layer_norm(values, gain):
    mean = jnp.mean(values, axis=-1, keepdims=True)
    centered = values - mean
    spread = jnp.mean(centered * centered, axis=-1, keepdims=True)
    return centered * lax.rsqrt(spread + 1e-06) * gain


def hidden_fold(rows, pieces):
    up_piece, down_piece = pieces
    hidden = jax.nn.gelu(
        jnp.dot(rows, up_piece, preferred_element_type=jnp.float32), approximate=False
    ).astype(jnp.bfloat16)
    return lax.dot_general(
        hidden, down_piece, (((1,), (1,)), ((), ())), preferred_element_type=jnp.float32
    )


def permute_gather(rows, axis):
    count = lax.axis_size(axis)
    here = lax.axis_index(axis)
    shifted = [rows] + [
        lax.ppermute(rows, axis, [(i, (i + s) % count) for i in range(count)])
        for s in range(1, count)
    ]
    stacked = jnp.stack(shifted)
    blocks = [
        lax.dynamic_index_in_dim(stacked, (here - source) % count, axis=0, keepdims=False)
        for source in range(count)
    ]
    return jnp.concatenate(blocks, axis=0)


def attend_block(
    queries,
    keys_blocked,
    values_blocked,
    images,
    images_blocked,
    first_row,
    q_block,
    k_block,
    scale,
):
    local_heads = keys_blocked.shape[2]
    query_part = queries[first_row : first_row + q_block].reshape(q_block, local_heads, HDIM)
    query_images = images[first_row : first_row + q_block]
    key_first = jnp.sum((images < images[first_row]).astype(jnp.int32))
    key_last = jnp.sum((images <= images[first_row + q_block - 1]).astype(jnp.int32))
    block_first = key_first // k_block
    block_last = (key_last + k_block - 1) // k_block

    def block_scores(kblock):
        scores = (
            jnp.einsum(
                "qhd,khd->hqk", query_part, keys_blocked[kblock], preferred_element_type=jnp.float32
            )
            * scale
        )
        same = query_images[:, None] == images_blocked[kblock][None, :]
        return jnp.where(same[None], scores, -1e30)

    def scan_stats(kblock, carry):
        row_max, row_sum = carry
        scores = block_scores(kblock)
        new_max = jnp.maximum(row_max, jnp.max(scores, axis=-1))
        row_sum = row_sum * jnp.exp(row_max - new_max) + jnp.sum(
            jnp.exp(scores - new_max[..., None]), axis=-1
        )
        return (new_max, row_sum)

    start_max = jnp.full((local_heads, q_block), -1e30, jnp.float32)
    start_sum = jnp.zeros((local_heads, q_block), jnp.float32)
    row_max, row_sum = lax.fori_loop(block_first, block_last, scan_stats, (start_max, start_sum))

    def add_values(kblock, totals):
        scores = block_scores(kblock)
        weights = (jnp.exp(scores - row_max[..., None]) / row_sum[..., None]).astype(jnp.bfloat16)
        return totals + jnp.einsum(
            "hqk,khd->qhd", weights, values_blocked[kblock], preferred_element_type=jnp.float32
        )

    totals = lax.fori_loop(
        block_first, block_last, add_values, jnp.zeros((q_block, local_heads, HDIM), jnp.float32)
    )
    return totals.reshape(q_block, local_heads * HDIM).astype(jnp.bfloat16)


def layer(tokens, segments, gain_attn, w_qkv, w_out, gain_mlp, w_up, w_down_t, gain_merge, w_proj):
    both = lax.all_gather(jnp.stack([w_up, w_down_t]), ("zx", "core", "tok"), axis=2, tiled=True)
    up_full, down_full = both[0], both[1]
    inputs = tokens.astype(jnp.float32)
    normed = layer_norm(inputs, gain_attn).astype(jnp.bfloat16)
    local_width = w_qkv.shape[2]
    joined = w_qkv.reshape(w_qkv.shape[0], 3 * local_width)
    stacked = jnp.dot(
        permute_gather(normed, "tok"),
        joined,
        preferred_element_type=jnp.float32,
    ).astype(jnp.bfloat16)
    group = stacked.shape[0]
    local_heads = local_width // HDIM
    q_block = min(512, group)
    k_block = min(128, group)
    scale = 1.0 / math.sqrt(HDIM)
    queries = stacked[:, :local_width]
    keys_blocked = stacked[:, local_width : 2 * local_width].reshape(
        group // k_block, k_block, local_heads, HDIM
    )
    values_blocked = stacked[:, 2 * local_width :].reshape(
        group // k_block, k_block, local_heads, HDIM
    )
    images = segments[0]
    images_blocked = images.reshape(group // k_block, k_block)
    outputs = []
    for block in range(group // q_block):
        outputs.append(
            attend_block(
                queries,
                keys_blocked,
                values_blocked,
                images,
                images_blocked,
                block * q_block,
                q_block,
                k_block,
                scale,
            )
        )
    heads_out = jnp.concatenate(outputs, axis=0)
    attended = lax.psum_scatter(
        jnp.dot(heads_out, w_out, preferred_element_type=jnp.float32).astype(jnp.bfloat16),
        "tok",
        scatter_dimension=0,
        tiled=True,
    ).astype(jnp.float32)
    first = (inputs + attended).astype(jnp.bfloat16)
    normed_mlp = layer_norm(first.astype(jnp.float32), gain_mlp).astype(jnp.bfloat16)
    mlp_out = hidden_fold(normed_mlp, (up_full, down_full))
    second = first.astype(jnp.float32) + mlp_out
    normed_merge = layer_norm(second, gain_merge).astype(jnp.bfloat16)
    merged = normed_merge.reshape(inputs.shape[0] // 4, 4 * inputs.shape[1])
    projected = jnp.dot(
        lax.all_gather(merged, "tok", axis=0, tiled=True),
        w_proj,
        preferred_element_type=jnp.float32,
    ).astype(jnp.bfloat16)
    return lax.all_to_all(projected, ("zx", "core"), split_axis=0, concat_axis=0, tiled=True)


def solution(mesh):
    devices = mesh.devices
    split = Mesh(devices.reshape(devices.shape[0] // 2, 2, devices.shape[1]), ("zx", "core", "tok"))
    rows = ("zx", "core")
    return jax.shard_map(
        layer,
        mesh=split,
        in_specs=(
            P(rows + ("tok",), None),
            P(rows, None),
            P(),
            P(None, None, "tok"),
            P("tok", None),
            P(),
            P(None, rows + ("tok",)),
            P(None, rows + ("tok",)),
            P(),
            P(None, "tok"),
        ),
        out_specs=P(rows, "tok"),
        check_vma=False,
    )
```

```python
import math

import jax
import jax.numpy as jnp
from jax import lax
from jax.sharding import Mesh, PartitionSpec as P


HDIM = 80


def layer_norm(values, gain):
    mean = jnp.mean(values, axis=-1, keepdims=True)
    centered = values - mean
    spread = jnp.mean(centered * centered, axis=-1, keepdims=True)
    return centered * lax.rsqrt(spread + 1e-06) * gain


def hidden_fold(rows, pieces):
    up_piece, down_piece = pieces
    hidden = jax.nn.gelu(
        jnp.dot(rows, up_piece, preferred_element_type=jnp.float32), approximate=False
    ).astype(jnp.bfloat16)
    return lax.dot_general(
        hidden, down_piece, (((1,), (1,)), ((), ())), preferred_element_type=jnp.float32
    )


def permute_gather(rows, axis):
    count = lax.axis_size(axis)
    here = lax.axis_index(axis)
    shifted = [rows] + [
        lax.ppermute(rows, axis, [(i, (i + s) % count) for i in range(count)])
        for s in range(1, count)
    ]
    stacked = jnp.stack(shifted)
    blocks = [
        lax.dynamic_index_in_dim(stacked, (here - source) % count, axis=0, keepdims=False)
        for source in range(count)
    ]
    return jnp.concatenate(blocks, axis=0)


def permute_scatter(parts, axis):
    count = lax.axis_size(axis)
    here = lax.axis_index(axis)
    blocks = parts.reshape(count, parts.shape[0] // count, parts.shape[1])
    total = lax.dynamic_index_in_dim(blocks, here, axis=0, keepdims=False).astype(jnp.float32)
    for s in range(1, count):
        outgoing = lax.dynamic_index_in_dim(blocks, (here + s) % count, axis=0, keepdims=False)
        incoming = lax.ppermute(outgoing, axis, [(i, (i + s) % count) for i in range(count)])
        total = total + incoming.astype(jnp.float32)
    return total


def attend_block(
    queries,
    keys_blocked,
    values_blocked,
    images,
    images_blocked,
    first_row,
    q_block,
    k_block,
    scale,
):
    local_heads = keys_blocked.shape[2]
    query_part = queries[first_row : first_row + q_block].reshape(q_block, local_heads, HDIM)
    query_images = images[first_row : first_row + q_block]
    key_first = jnp.sum((images < images[first_row]).astype(jnp.int32))
    key_last = jnp.sum((images <= images[first_row + q_block - 1]).astype(jnp.int32))
    block_first = key_first // k_block
    block_last = (key_last + k_block - 1) // k_block

    def block_scores(kblock):
        scores = (
            jnp.einsum(
                "qhd,khd->hqk", query_part, keys_blocked[kblock], preferred_element_type=jnp.float32
            )
            * scale
        )
        same = query_images[:, None] == images_blocked[kblock][None, :]
        return jnp.where(same[None], scores, -1e30)

    def scan_stats(kblock, carry):
        row_max, row_sum = carry
        scores = block_scores(kblock)
        new_max = jnp.maximum(row_max, jnp.max(scores, axis=-1))
        row_sum = row_sum * jnp.exp(row_max - new_max) + jnp.sum(
            jnp.exp(scores - new_max[..., None]), axis=-1
        )
        return (new_max, row_sum)

    start_max = jnp.full((local_heads, q_block), -1e30, jnp.float32)
    start_sum = jnp.zeros((local_heads, q_block), jnp.float32)
    row_max, row_sum = lax.fori_loop(block_first, block_last, scan_stats, (start_max, start_sum))

    def add_values(kblock, totals):
        scores = block_scores(kblock)
        weights = (jnp.exp(scores - row_max[..., None]) / row_sum[..., None]).astype(jnp.bfloat16)
        return totals + jnp.einsum(
            "hqk,khd->qhd", weights, values_blocked[kblock], preferred_element_type=jnp.float32
        )

    totals = lax.fori_loop(
        block_first, block_last, add_values, jnp.zeros((q_block, local_heads, HDIM), jnp.float32)
    )
    return totals.reshape(q_block, local_heads * HDIM).astype(jnp.bfloat16)


def layer(tokens, segments, gain_attn, w_qkv, w_out, gain_mlp, w_up, w_down_t, gain_merge, w_proj):
    both = lax.all_gather(jnp.stack([w_up, w_down_t]), ("zx", "tok"), axis=2, tiled=True)
    up_full, down_full = both[0], both[1]
    inputs = tokens.astype(jnp.float32)
    normed = layer_norm(inputs, gain_attn).astype(jnp.bfloat16)
    local_width = w_qkv.shape[2]
    joined = w_qkv.reshape(w_qkv.shape[0], 3 * local_width)
    stacked = jnp.dot(
        permute_gather(normed, "tok"),
        joined,
        preferred_element_type=jnp.float32,
    ).astype(jnp.bfloat16)
    group = stacked.shape[0]
    local_heads = local_width // HDIM
    q_block = min(512, group)
    k_block = min(128, group)
    scale = 1.0 / math.sqrt(HDIM)
    queries = stacked[:, :local_width]
    keys_blocked = stacked[:, local_width : 2 * local_width].reshape(
        group // k_block, k_block, local_heads, HDIM
    )
    values_blocked = stacked[:, 2 * local_width :].reshape(
        group // k_block, k_block, local_heads, HDIM
    )
    images = segments[0]
    images_blocked = images.reshape(group // k_block, k_block)
    outputs = []
    for block in range(group // q_block):
        outputs.append(
            attend_block(
                queries,
                keys_blocked,
                values_blocked,
                images,
                images_blocked,
                block * q_block,
                q_block,
                k_block,
                scale,
            )
        )
    heads_out = jnp.concatenate(outputs, axis=0)
    attended = permute_scatter(
        jnp.dot(heads_out, w_out, preferred_element_type=jnp.float32).astype(jnp.bfloat16),
        "tok",
    )
    first = (inputs + attended).astype(jnp.bfloat16)
    normed_mlp = layer_norm(first.astype(jnp.float32), gain_mlp).astype(jnp.bfloat16)
    mlp_out = permute_scatter(
        hidden_fold(permute_gather(normed_mlp, "core"), (up_full, down_full)), "core"
    )
    second = first.astype(jnp.float32) + mlp_out
    normed_merge = layer_norm(second, gain_merge).astype(jnp.bfloat16)
    merged = normed_merge.reshape(inputs.shape[0] // 4, 4 * inputs.shape[1])
    projected = jnp.dot(
        lax.all_gather(merged, "tok", axis=0, tiled=True),
        w_proj,
        preferred_element_type=jnp.float32,
    ).astype(jnp.bfloat16)
    return lax.all_to_all(projected, ("zx", "core"), split_axis=0, concat_axis=0, tiled=True)


def solution(mesh):
    devices = mesh.devices
    split = Mesh(devices.reshape(devices.shape[0] // 2, 2, devices.shape[1]), ("zx", "core", "tok"))
    rows = ("zx", "core")
    return jax.shard_map(
        layer,
        mesh=split,
        in_specs=(
            P(rows + ("tok",), None),
            P(rows, None),
            P(),
            P(None, None, "tok"),
            P("tok", None),
            P(),
            P(None, rows + ("tok",)),
            P(None, rows + ("tok",)),
            P(),
            P(None, "tok"),
        ),
        out_specs=P(rows, "tok"),
        check_vma=False,
    )
```

```python
import math

import jax
import jax.numpy as jnp
from jax import lax
from jax.sharding import Mesh, PartitionSpec as P


HDIM = 80


def layer_norm(values, gain):
    mean = jnp.mean(values, axis=-1, keepdims=True)
    centered = values - mean
    spread = jnp.mean(centered * centered, axis=-1, keepdims=True)
    return centered * lax.rsqrt(spread + 1e-06) * gain


def hidden_fold(rows, pieces):
    up_piece, down_piece = pieces
    hidden = jax.nn.gelu(
        jnp.dot(rows, up_piece, preferred_element_type=jnp.float32), approximate=False
    ).astype(jnp.bfloat16)
    return lax.dot_general(
        hidden, down_piece, (((1,), (1,)), ((), ())), preferred_element_type=jnp.float32
    )


def permute_gather(rows, axis):
    count = lax.axis_size(axis)
    here = lax.axis_index(axis)
    shifted = [rows] + [
        lax.ppermute(rows, axis, [(i, (i + s) % count) for i in range(count)])
        for s in range(1, count)
    ]
    stacked = jnp.stack(shifted)
    blocks = [
        lax.dynamic_index_in_dim(stacked, (here - source) % count, axis=0, keepdims=False)
        for source in range(count)
    ]
    return jnp.concatenate(blocks, axis=0)


def permute_scatter(parts, axis):
    count = lax.axis_size(axis)
    here = lax.axis_index(axis)
    blocks = parts.reshape(count, parts.shape[0] // count, parts.shape[1])
    total = lax.dynamic_index_in_dim(blocks, here, axis=0, keepdims=False).astype(jnp.float32)
    for s in range(1, count):
        outgoing = lax.dynamic_index_in_dim(blocks, (here + s) % count, axis=0, keepdims=False)
        incoming = lax.ppermute(outgoing, axis, [(i, (i + s) % count) for i in range(count)])
        total = total + incoming.astype(jnp.float32)
    return total


def attend_block(
    queries,
    keys_blocked,
    values_blocked,
    images,
    images_blocked,
    first_row,
    q_block,
    k_block,
    scale,
):
    local_heads = keys_blocked.shape[2]
    query_part = queries[first_row : first_row + q_block].reshape(q_block, local_heads, HDIM)
    query_images = images[first_row : first_row + q_block]
    key_first = jnp.sum((images < images[first_row]).astype(jnp.int32))
    key_last = jnp.sum((images <= images[first_row + q_block - 1]).astype(jnp.int32))
    block_first = key_first // k_block
    block_last = (key_last + k_block - 1) // k_block

    def block_scores(kblock):
        scores = (
            jnp.einsum(
                "qhd,khd->hqk", query_part, keys_blocked[kblock], preferred_element_type=jnp.float32
            )
            * scale
        )
        same = query_images[:, None] == images_blocked[kblock][None, :]
        return jnp.where(same[None], scores, -1e30)

    def scan_stats(kblock, carry):
        row_max, row_sum = carry
        scores = block_scores(kblock)
        new_max = jnp.maximum(row_max, jnp.max(scores, axis=-1))
        row_sum = row_sum * jnp.exp(row_max - new_max) + jnp.sum(
            jnp.exp(scores - new_max[..., None]), axis=-1
        )
        return (new_max, row_sum)

    start_max = jnp.full((local_heads, q_block), -1e30, jnp.float32)
    start_sum = jnp.zeros((local_heads, q_block), jnp.float32)
    row_max, row_sum = lax.fori_loop(block_first, block_last, scan_stats, (start_max, start_sum))

    def add_values(kblock, totals):
        scores = block_scores(kblock)
        weights = (jnp.exp(scores - row_max[..., None]) / row_sum[..., None]).astype(jnp.bfloat16)
        return totals + jnp.einsum(
            "hqk,khd->qhd", weights, values_blocked[kblock], preferred_element_type=jnp.float32
        )

    totals = lax.fori_loop(
        block_first, block_last, add_values, jnp.zeros((q_block, local_heads, HDIM), jnp.float32)
    )
    return totals.reshape(q_block, local_heads * HDIM).astype(jnp.bfloat16)


def layer(tokens, segments, gain_attn, w_qkv, w_out, gain_mlp, w_up, w_down_t, gain_merge, w_proj):
    both = lax.all_gather(jnp.stack([w_up, w_down_t]), ("zx", "core", "tok"), axis=2, tiled=True)
    up_full, down_full = both[0], both[1]
    inputs = tokens.astype(jnp.float32)
    normed = layer_norm(inputs, gain_attn).astype(jnp.bfloat16)
    local_width = w_qkv.shape[2]
    joined = w_qkv.reshape(w_qkv.shape[0], 3 * local_width)
    stacked = jnp.dot(
        permute_gather(normed, "tok"),
        joined,
        preferred_element_type=jnp.float32,
    ).astype(jnp.bfloat16)
    group = stacked.shape[0]
    local_heads = local_width // HDIM
    q_block = min(512, group)
    k_block = min(128, group)
    scale = 1.0 / math.sqrt(HDIM)
    queries = stacked[:, :local_width]
    keys_blocked = stacked[:, local_width : 2 * local_width].reshape(
        group // k_block, k_block, local_heads, HDIM
    )
    values_blocked = stacked[:, 2 * local_width :].reshape(
        group // k_block, k_block, local_heads, HDIM
    )
    images = segments[0]
    images_blocked = images.reshape(group // k_block, k_block)
    outputs = []
    for block in range(group // q_block):
        outputs.append(
            attend_block(
                queries,
                keys_blocked,
                values_blocked,
                images,
                images_blocked,
                block * q_block,
                q_block,
                k_block,
                scale,
            )
        )
    heads_out = jnp.concatenate(outputs, axis=0)
    attended = permute_scatter(
        jnp.dot(heads_out, w_out, preferred_element_type=jnp.float32).astype(jnp.bfloat16),
        "tok",
    )
    first = (inputs + attended).astype(jnp.bfloat16)
    normed_mlp = layer_norm(first.astype(jnp.float32), gain_mlp).astype(jnp.bfloat16)
    mlp_out = hidden_fold(normed_mlp, (up_full, down_full))
    second = first.astype(jnp.float32) + mlp_out
    normed_merge = layer_norm(second, gain_merge).astype(jnp.bfloat16)
    merged = normed_merge.reshape(inputs.shape[0] // 4, 4 * inputs.shape[1])
    projected = jnp.dot(
        permute_gather(merged, "tok"),
        w_proj,
        preferred_element_type=jnp.float32,
    ).astype(jnp.bfloat16)
    return lax.all_to_all(projected, ("zx", "core"), split_axis=0, concat_axis=0, tiled=True)


def solution(mesh):
    devices = mesh.devices
    split = Mesh(devices.reshape(devices.shape[0] // 2, 2, devices.shape[1]), ("zx", "core", "tok"))
    rows = ("zx", "core")
    return jax.shard_map(
        layer,
        mesh=split,
        in_specs=(
            P(rows + ("tok",), None),
            P(rows, None),
            P(),
            P(None, None, "tok"),
            P("tok", None),
            P(),
            P(None, rows + ("tok",)),
            P(None, rows + ("tok",)),
            P(),
            P(None, "tok"),
        ),
        out_specs=P(rows, "tok"),
        check_vma=False,
    )
```

```python
import math

import jax
import jax.numpy as jnp
from jax import lax
from jax.sharding import Mesh, PartitionSpec as P


HDIM = 80


def layer_norm(values, gain):
    mean = jnp.mean(values, axis=-1, keepdims=True)
    centered = values - mean
    spread = jnp.mean(centered * centered, axis=-1, keepdims=True)
    return centered * lax.rsqrt(spread + 1e-06) * gain


def hidden_fold(rows, pieces):
    up_piece, down_piece = pieces
    hidden = jax.nn.gelu(
        jnp.dot(rows, up_piece, preferred_element_type=jnp.float32), approximate=False
    ).astype(jnp.bfloat16)
    return lax.dot_general(
        hidden, down_piece, (((1,), (1,)), ((), ())), preferred_element_type=jnp.float32
    )


def permute_gather(rows, axis):
    count = lax.axis_size(axis)
    here = lax.axis_index(axis)
    shifted = [rows] + [
        lax.ppermute(rows, axis, [(i, (i + s) % count) for i in range(count)])
        for s in range(1, count)
    ]
    stacked = jnp.stack(shifted)
    blocks = [
        lax.dynamic_index_in_dim(stacked, (here - source) % count, axis=0, keepdims=False)
        for source in range(count)
    ]
    return jnp.concatenate(blocks, axis=0)


def permute_scatter(parts, axis):
    count = lax.axis_size(axis)
    here = lax.axis_index(axis)
    blocks = parts.reshape(count, parts.shape[0] // count, parts.shape[1])
    total = lax.dynamic_index_in_dim(blocks, here, axis=0, keepdims=False).astype(jnp.float32)
    for s in range(1, count):
        outgoing = lax.dynamic_index_in_dim(blocks, (here + s) % count, axis=0, keepdims=False)
        incoming = lax.ppermute(outgoing, axis, [(i, (i + s) % count) for i in range(count)])
        total = total + incoming.astype(jnp.float32)
    return total


def permute_exchange(rows, axes):
    count = 1
    for axis in axes:
        count *= lax.axis_size(axis)
    here = lax.axis_index(axes)
    blocks = rows.reshape(count, rows.shape[0] // count, rows.shape[1])
    received = [lax.dynamic_index_in_dim(blocks, here, axis=0, keepdims=False)]
    for s in range(1, count):
        outgoing = lax.dynamic_index_in_dim(blocks, (here + s) % count, axis=0, keepdims=False)
        received.append(lax.ppermute(outgoing, axes, [(i, (i + s) % count) for i in range(count)]))
    order = (here - jnp.arange(count)) % count
    return jnp.take(jnp.stack(received), order, axis=0).reshape(rows.shape)


def attend_block(
    queries,
    keys_blocked,
    values_blocked,
    images,
    images_blocked,
    first_row,
    q_block,
    k_block,
    scale,
):
    local_heads = keys_blocked.shape[2]
    query_part = queries[first_row : first_row + q_block].reshape(q_block, local_heads, HDIM)
    query_images = images[first_row : first_row + q_block]
    key_first = jnp.sum((images < images[first_row]).astype(jnp.int32))
    key_last = jnp.sum((images <= images[first_row + q_block - 1]).astype(jnp.int32))
    block_first = key_first // k_block
    block_last = (key_last + k_block - 1) // k_block

    def block_scores(kblock):
        scores = (
            jnp.einsum(
                "qhd,khd->hqk", query_part, keys_blocked[kblock], preferred_element_type=jnp.float32
            )
            * scale
        )
        same = query_images[:, None] == images_blocked[kblock][None, :]
        return jnp.where(same[None], scores, -1e30)

    def scan_stats(kblock, carry):
        row_max, row_sum = carry
        scores = block_scores(kblock)
        new_max = jnp.maximum(row_max, jnp.max(scores, axis=-1))
        row_sum = row_sum * jnp.exp(row_max - new_max) + jnp.sum(
            jnp.exp(scores - new_max[..., None]), axis=-1
        )
        return (new_max, row_sum)

    start_max = jnp.full((local_heads, q_block), -1e30, jnp.float32)
    start_sum = jnp.zeros((local_heads, q_block), jnp.float32)
    row_max, row_sum = lax.fori_loop(block_first, block_last, scan_stats, (start_max, start_sum))

    def add_values(kblock, totals):
        scores = block_scores(kblock)
        weights = (jnp.exp(scores - row_max[..., None]) / row_sum[..., None]).astype(jnp.bfloat16)
        return totals + jnp.einsum(
            "hqk,khd->qhd", weights, values_blocked[kblock], preferred_element_type=jnp.float32
        )

    totals = lax.fori_loop(
        block_first, block_last, add_values, jnp.zeros((q_block, local_heads, HDIM), jnp.float32)
    )
    return totals.reshape(q_block, local_heads * HDIM).astype(jnp.bfloat16)


def layer(tokens, segments, gain_attn, w_qkv, w_out, gain_mlp, w_up, w_down_t, gain_merge, w_proj):
    both = lax.all_gather(jnp.stack([w_up, w_down_t]), ("zx", "core", "tok"), axis=2, tiled=True)
    up_full, down_full = both[0], both[1]
    inputs = tokens.astype(jnp.float32)
    normed = layer_norm(inputs, gain_attn).astype(jnp.bfloat16)
    local_width = w_qkv.shape[2]
    joined = w_qkv.reshape(w_qkv.shape[0], 3 * local_width)
    stacked = jnp.dot(
        permute_gather(normed, "tok"),
        joined,
        preferred_element_type=jnp.float32,
    ).astype(jnp.bfloat16)
    group = stacked.shape[0]
    local_heads = local_width // HDIM
    q_block = min(512, group)
    k_block = min(128, group)
    scale = 1.0 / math.sqrt(HDIM)
    queries = stacked[:, :local_width]
    keys_blocked = stacked[:, local_width : 2 * local_width].reshape(
        group // k_block, k_block, local_heads, HDIM
    )
    values_blocked = stacked[:, 2 * local_width :].reshape(
        group // k_block, k_block, local_heads, HDIM
    )
    images = segments[0]
    images_blocked = images.reshape(group // k_block, k_block)
    outputs = []
    for block in range(group // q_block):
        outputs.append(
            attend_block(
                queries,
                keys_blocked,
                values_blocked,
                images,
                images_blocked,
                block * q_block,
                q_block,
                k_block,
                scale,
            )
        )
    heads_out = jnp.concatenate(outputs, axis=0)
    attended = permute_scatter(
        jnp.dot(heads_out, w_out, preferred_element_type=jnp.float32).astype(jnp.bfloat16),
        "tok",
    )
    first = (inputs + attended).astype(jnp.bfloat16)
    normed_mlp = layer_norm(first.astype(jnp.float32), gain_mlp).astype(jnp.bfloat16)
    mlp_out = hidden_fold(normed_mlp, (up_full, down_full))
    second = first.astype(jnp.float32) + mlp_out
    normed_merge = layer_norm(second, gain_merge).astype(jnp.bfloat16)
    merged = normed_merge.reshape(inputs.shape[0] // 4, 4 * inputs.shape[1])
    projected = jnp.dot(
        permute_gather(merged, "tok"),
        w_proj,
        preferred_element_type=jnp.float32,
    ).astype(jnp.bfloat16)
    return permute_exchange(projected, ("zx", "core"))


def solution(mesh):
    devices = mesh.devices
    split = Mesh(devices.reshape(devices.shape[0] // 2, 2, devices.shape[1]), ("zx", "core", "tok"))
    rows = ("zx", "core")
    return jax.shard_map(
        layer,
        mesh=split,
        in_specs=(
            P(rows + ("tok",), None),
            P(rows, None),
            P(),
            P(None, None, "tok"),
            P("tok", None),
            P(),
            P(None, rows + ("tok",)),
            P(None, rows + ("tok",)),
            P(),
            P(None, "tok"),
        ),
        out_specs=P(rows, "tok"),
        check_vma=False,
    )
```

```python
import math

import jax
import jax.numpy as jnp
from jax import lax
from jax.sharding import Mesh, PartitionSpec as P


HDIM = 80


def layer_norm(values, gain):
    mean = jnp.mean(values, axis=-1, keepdims=True)
    centered = values - mean
    spread = jnp.mean(centered * centered, axis=-1, keepdims=True)
    return centered * lax.rsqrt(spread + 1e-06) * gain


def hidden_fold(rows, pieces):
    up_piece, down_piece = pieces
    hidden = jax.nn.gelu(
        jnp.dot(rows, up_piece, preferred_element_type=jnp.float32), approximate=False
    ).astype(jnp.bfloat16)
    return lax.dot_general(
        hidden, down_piece, (((1,), (1,)), ((), ())), preferred_element_type=jnp.float32
    )


def permute_gather(rows, axis):
    count = lax.axis_size(axis)
    here = lax.axis_index(axis)
    shifted = [rows] + [
        lax.ppermute(rows, axis, [(i, (i + s) % count) for i in range(count)])
        for s in range(1, count)
    ]
    stacked = jnp.stack(shifted)
    blocks = [
        lax.dynamic_index_in_dim(stacked, (here - source) % count, axis=0, keepdims=False)
        for source in range(count)
    ]
    return jnp.concatenate(blocks, axis=0)


def permute_scatter(parts, axis):
    count = lax.axis_size(axis)
    here = lax.axis_index(axis)
    blocks = parts.reshape(count, parts.shape[0] // count, parts.shape[1])
    total = lax.dynamic_index_in_dim(blocks, here, axis=0, keepdims=False).astype(jnp.float32)
    for s in range(1, count):
        outgoing = lax.dynamic_index_in_dim(blocks, (here + s) % count, axis=0, keepdims=False)
        incoming = lax.ppermute(outgoing, axis, [(i, (i + s) % count) for i in range(count)])
        total = total + incoming.astype(jnp.float32)
    return total


def attend_block(
    queries,
    keys_blocked,
    values_blocked,
    images,
    images_blocked,
    first_row,
    q_block,
    k_block,
    scale,
):
    local_heads = keys_blocked.shape[2]
    query_part = queries[first_row : first_row + q_block].reshape(q_block, local_heads, HDIM)
    query_images = images[first_row : first_row + q_block]
    key_first = jnp.sum((images < images[first_row]).astype(jnp.int32))
    key_last = jnp.sum((images <= images[first_row + q_block - 1]).astype(jnp.int32))
    block_first = key_first // k_block
    block_last = (key_last + k_block - 1) // k_block

    def block_scores(kblock):
        scores = (
            jnp.einsum(
                "qhd,khd->hqk", query_part, keys_blocked[kblock], preferred_element_type=jnp.float32
            )
            * scale
        )
        same = query_images[:, None] == images_blocked[kblock][None, :]
        return jnp.where(same[None], scores, -1e30)

    def scan_stats(kblock, carry):
        row_max, row_sum = carry
        scores = block_scores(kblock)
        new_max = jnp.maximum(row_max, jnp.max(scores, axis=-1))
        row_sum = row_sum * jnp.exp(row_max - new_max) + jnp.sum(
            jnp.exp(scores - new_max[..., None]), axis=-1
        )
        return (new_max, row_sum)

    start_max = jnp.full((local_heads, q_block), -1e30, jnp.float32)
    start_sum = jnp.zeros((local_heads, q_block), jnp.float32)
    row_max, row_sum = lax.fori_loop(block_first, block_last, scan_stats, (start_max, start_sum))

    def add_values(kblock, totals):
        scores = block_scores(kblock)
        weights = (jnp.exp(scores - row_max[..., None]) / row_sum[..., None]).astype(jnp.bfloat16)
        return totals + jnp.einsum(
            "hqk,khd->qhd", weights, values_blocked[kblock], preferred_element_type=jnp.float32
        )

    totals = lax.fori_loop(
        block_first, block_last, add_values, jnp.zeros((q_block, local_heads, HDIM), jnp.float32)
    )
    return totals.reshape(q_block, local_heads * HDIM).astype(jnp.bfloat16)


def layer(tokens, segments, gain_attn, w_qkv, w_out, gain_mlp, w_up, w_down_t, gain_merge, w_proj):
    both = lax.all_gather(jnp.stack([w_up, w_down_t]), ("zx", "core", "tok"), axis=2, tiled=True)
    up_full, down_full = both[0], both[1]
    inputs = tokens.astype(jnp.float32)
    normed = layer_norm(inputs, gain_attn).astype(jnp.bfloat16)
    local_width = w_qkv.shape[2]
    joined = w_qkv.reshape(w_qkv.shape[0], 3 * local_width)
    stacked = jnp.dot(
        permute_gather(normed, "tok"),
        joined,
        preferred_element_type=jnp.float32,
    ).astype(jnp.bfloat16)
    group = stacked.shape[0]
    local_heads = local_width // HDIM
    q_block = min(512, group)
    k_block = min(128, group)
    scale = 1.0 / math.sqrt(HDIM)
    queries = stacked[:, :local_width]
    keys_blocked = stacked[:, local_width : 2 * local_width].reshape(
        group // k_block, k_block, local_heads, HDIM
    )
    values_blocked = stacked[:, 2 * local_width :].reshape(
        group // k_block, k_block, local_heads, HDIM
    )
    images = segments[0]
    images_blocked = images.reshape(group // k_block, k_block)
    outputs = []
    for block in range(group // q_block):
        outputs.append(
            attend_block(
                queries,
                keys_blocked,
                values_blocked,
                images,
                images_blocked,
                block * q_block,
                q_block,
                k_block,
                scale,
            )
        )
    heads_out = jnp.concatenate(outputs, axis=0)
    attended = permute_scatter(
        jnp.dot(heads_out, w_out, preferred_element_type=jnp.float32).astype(jnp.bfloat16),
        "tok",
    )
    first = (inputs + attended).astype(jnp.bfloat16)
    normed_mlp = layer_norm(first.astype(jnp.float32), gain_mlp).astype(jnp.bfloat16)
    mlp_out = hidden_fold(normed_mlp, (up_full, down_full))
    second = first.astype(jnp.float32) + mlp_out
    normed_merge = layer_norm(second, gain_merge).astype(jnp.bfloat16)
    merged = normed_merge.reshape(inputs.shape[0] // 4, 4 * inputs.shape[1])
    projected = jnp.dot(
        permute_gather(merged, "tok"),
        w_proj,
        preferred_element_type=jnp.float32,
    ).astype(jnp.bfloat16)
    zx, core = lax.axis_size("zx"), lax.axis_size("core")
    blocks = projected.reshape(zx, core, projected.shape[0] // (zx * core), projected.shape[1])
    blocks = lax.all_to_all(blocks, "core", split_axis=1, concat_axis=1, tiled=True)
    blocks = lax.all_to_all(blocks, "zx", split_axis=0, concat_axis=0, tiled=True)
    return blocks.reshape(projected.shape)


def solution(mesh):
    devices = mesh.devices
    split = Mesh(devices.reshape(devices.shape[0] // 2, 2, devices.shape[1]), ("zx", "core", "tok"))
    rows = ("zx", "core")
    return jax.shard_map(
        layer,
        mesh=split,
        in_specs=(
            P(rows + ("tok",), None),
            P(rows, None),
            P(),
            P(None, None, "tok"),
            P("tok", None),
            P(),
            P(None, rows + ("tok",)),
            P(None, rows + ("tok",)),
            P(),
            P(None, "tok"),
        ),
        out_specs=P(rows, "tok"),
        check_vma=False,
    )
```

```python
import math

import jax
import jax.numpy as jnp
from jax import lax
from jax.sharding import Mesh, PartitionSpec as P


HDIM = 80


def layer_norm(values, gain):
    mean = jnp.mean(values, axis=-1, keepdims=True)
    centered = values - mean
    spread = jnp.mean(centered * centered, axis=-1, keepdims=True)
    return centered * lax.rsqrt(spread + 1e-06) * gain


def hidden_fold(rows, pieces):
    up_piece, down_piece = pieces
    hidden = jax.nn.gelu(
        jnp.dot(rows, up_piece, preferred_element_type=jnp.float32), approximate=False
    ).astype(jnp.bfloat16)
    return lax.dot_general(
        hidden, down_piece, (((1,), (1,)), ((), ())), preferred_element_type=jnp.float32
    )


def permute_gather(rows, axis, each=lambda rows: rows):
    count = lax.axis_size(axis)
    here = lax.axis_index(axis)
    shifted = [each(rows)] + [
        each(lax.ppermute(rows, axis, [(i, (i + s) % count) for i in range(count)]))
        for s in range(1, count)
    ]
    stacked = jnp.stack(shifted)
    blocks = [
        lax.dynamic_index_in_dim(stacked, (here - source) % count, axis=0, keepdims=False)
        for source in range(count)
    ]
    return jnp.concatenate(blocks, axis=0)


def permute_scatter(parts, axis):
    count = lax.axis_size(axis)
    here = lax.axis_index(axis)
    blocks = parts.reshape(count, parts.shape[0] // count, parts.shape[1])
    total = lax.dynamic_index_in_dim(blocks, here, axis=0, keepdims=False).astype(jnp.float32)
    for s in range(1, count):
        outgoing = lax.dynamic_index_in_dim(blocks, (here + s) % count, axis=0, keepdims=False)
        incoming = lax.ppermute(outgoing, axis, [(i, (i + s) % count) for i in range(count)])
        total = total + incoming.astype(jnp.float32)
    return total


def attend_block(
    queries,
    keys_blocked,
    values_blocked,
    images,
    images_blocked,
    first_row,
    q_block,
    k_block,
    scale,
):
    local_heads = keys_blocked.shape[2]
    query_part = queries[first_row : first_row + q_block].reshape(q_block, local_heads, HDIM)
    query_images = images[first_row : first_row + q_block]
    key_first = jnp.sum((images < images[first_row]).astype(jnp.int32))
    key_last = jnp.sum((images <= images[first_row + q_block - 1]).astype(jnp.int32))
    block_first = key_first // k_block
    block_last = (key_last + k_block - 1) // k_block

    def block_scores(kblock):
        scores = (
            jnp.einsum(
                "qhd,khd->hqk", query_part, keys_blocked[kblock], preferred_element_type=jnp.float32
            )
            * scale
        )
        same = query_images[:, None] == images_blocked[kblock][None, :]
        return jnp.where(same[None], scores, -1e30)

    def scan_stats(kblock, carry):
        row_max, row_sum = carry
        scores = block_scores(kblock)
        new_max = jnp.maximum(row_max, jnp.max(scores, axis=-1))
        row_sum = row_sum * jnp.exp(row_max - new_max) + jnp.sum(
            jnp.exp(scores - new_max[..., None]), axis=-1
        )
        return (new_max, row_sum)

    start_max = jnp.full((local_heads, q_block), -1e30, jnp.float32)
    start_sum = jnp.zeros((local_heads, q_block), jnp.float32)
    row_max, row_sum = lax.fori_loop(block_first, block_last, scan_stats, (start_max, start_sum))

    def add_values(kblock, totals):
        scores = block_scores(kblock)
        weights = (jnp.exp(scores - row_max[..., None]) / row_sum[..., None]).astype(jnp.bfloat16)
        return totals + jnp.einsum(
            "hqk,khd->qhd", weights, values_blocked[kblock], preferred_element_type=jnp.float32
        )

    totals = lax.fori_loop(
        block_first, block_last, add_values, jnp.zeros((q_block, local_heads, HDIM), jnp.float32)
    )
    return totals.reshape(q_block, local_heads * HDIM).astype(jnp.bfloat16)


def layer(tokens, segments, gain_attn, w_qkv, w_out, gain_mlp, w_up, w_down_t, gain_merge, w_proj):
    both = lax.all_gather(jnp.stack([w_up, w_down_t]), ("zx", "core", "tok"), axis=2, tiled=True)
    up_full, down_full = both[0], both[1]
    inputs = tokens.astype(jnp.float32)
    normed = layer_norm(inputs, gain_attn).astype(jnp.bfloat16)
    local_width = w_qkv.shape[2]
    joined = w_qkv.reshape(w_qkv.shape[0], 3 * local_width)
    stacked = jnp.dot(
        permute_gather(normed, "tok"),
        joined,
        preferred_element_type=jnp.float32,
    ).astype(jnp.bfloat16)
    group = stacked.shape[0]
    local_heads = local_width // HDIM
    q_block = min(512, group)
    k_block = min(128, group)
    scale = 1.0 / math.sqrt(HDIM)
    queries = stacked[:, :local_width]
    keys_blocked = stacked[:, local_width : 2 * local_width].reshape(
        group // k_block, k_block, local_heads, HDIM
    )
    values_blocked = stacked[:, 2 * local_width :].reshape(
        group // k_block, k_block, local_heads, HDIM
    )
    images = segments[0]
    images_blocked = images.reshape(group // k_block, k_block)
    outputs = []
    for block in range(group // q_block):
        outputs.append(
            attend_block(
                queries,
                keys_blocked,
                values_blocked,
                images,
                images_blocked,
                block * q_block,
                q_block,
                k_block,
                scale,
            )
        )
    heads_out = jnp.concatenate(outputs, axis=0)
    attended = permute_scatter(
        jnp.dot(heads_out, w_out, preferred_element_type=jnp.float32).astype(jnp.bfloat16),
        "tok",
    )
    first = (inputs + attended).astype(jnp.bfloat16)
    normed_mlp = layer_norm(first.astype(jnp.float32), gain_mlp).astype(jnp.bfloat16)
    mlp_out = hidden_fold(normed_mlp, (up_full, down_full))
    second = first.astype(jnp.float32) + mlp_out
    normed_merge = layer_norm(second, gain_merge).astype(jnp.bfloat16)
    merged = normed_merge.reshape(inputs.shape[0] // 4, 4 * inputs.shape[1])
    projected = permute_gather(
        merged,
        "tok",
        lambda rows: jnp.dot(rows, w_proj, preferred_element_type=jnp.float32).astype(jnp.bfloat16),
    )
    return lax.all_to_all(projected, ("zx", "core"), split_axis=0, concat_axis=0, tiled=True)


def solution(mesh):
    devices = mesh.devices
    split = Mesh(devices.reshape(devices.shape[0] // 2, 2, devices.shape[1]), ("zx", "core", "tok"))
    rows = ("zx", "core")
    return jax.shard_map(
        layer,
        mesh=split,
        in_specs=(
            P(rows + ("tok",), None),
            P(rows, None),
            P(),
            P(None, None, "tok"),
            P("tok", None),
            P(),
            P(None, rows + ("tok",)),
            P(None, rows + ("tok",)),
            P(),
            P(None, "tok"),
        ),
        out_specs=P(rows, "tok"),
        check_vma=False,
    )
```

```python
import math

import jax
import jax.numpy as jnp
from jax import lax
from jax.sharding import Mesh, PartitionSpec as P


HDIM = 80


def layer_norm(values, gain):
    mean = jnp.mean(values, axis=-1, keepdims=True)
    centered = values - mean
    spread = jnp.mean(centered * centered, axis=-1, keepdims=True)
    return centered * lax.rsqrt(spread + 1e-06) * gain


def hidden_fold(rows, pieces):
    up_piece, down_piece = pieces
    hidden = jax.nn.gelu(
        jnp.dot(rows, up_piece, preferred_element_type=jnp.float32), approximate=False
    ).astype(jnp.bfloat16)
    return lax.dot_general(
        hidden, down_piece, (((1,), (1,)), ((), ())), preferred_element_type=jnp.float32
    )


def shift(rows, axis, count, s):
    return lax.ppermute(rows, axis, [(i, (i + s) % count) for i in range(count)])


def shift_rows(rows, axis, count, s):
    if count != 4 or s != 2:
        return shift(rows, axis, count, s)
    half = rows.shape[0] // 2
    ahead = shift(rows[:half], axis, count, 2)
    behind = shift(shift(rows[half:], axis, count, -1), axis, count, -1)
    return jnp.concatenate([ahead, behind], axis=0)


def permute_gather(rows, axis):
    count = lax.axis_size(axis)
    here = lax.axis_index(axis)
    shifted = [rows] + [shift_rows(rows, axis, count, s) for s in range(1, count)]
    stacked = jnp.stack(shifted)
    blocks = [
        lax.dynamic_index_in_dim(stacked, (here - source) % count, axis=0, keepdims=False)
        for source in range(count)
    ]
    return jnp.concatenate(blocks, axis=0)


def permute_scatter(parts, axis):
    count = lax.axis_size(axis)
    here = lax.axis_index(axis)
    blocks = parts.reshape(count, parts.shape[0] // count, parts.shape[1])
    total = lax.dynamic_index_in_dim(blocks, here, axis=0, keepdims=False).astype(jnp.float32)
    for s in range(1, count):
        outgoing = lax.dynamic_index_in_dim(blocks, (here + s) % count, axis=0, keepdims=False)
        incoming = shift_rows(outgoing, axis, count, s)
        total = total + incoming.astype(jnp.float32)
    return total


def attend_block(
    queries,
    keys_blocked,
    values_blocked,
    images,
    images_blocked,
    first_row,
    q_block,
    k_block,
    scale,
):
    local_heads = keys_blocked.shape[2]
    query_part = queries[first_row : first_row + q_block].reshape(q_block, local_heads, HDIM)
    query_images = images[first_row : first_row + q_block]
    key_first = jnp.sum((images < images[first_row]).astype(jnp.int32))
    key_last = jnp.sum((images <= images[first_row + q_block - 1]).astype(jnp.int32))
    block_first = key_first // k_block
    block_last = (key_last + k_block - 1) // k_block

    def block_scores(kblock):
        scores = (
            jnp.einsum(
                "qhd,khd->hqk", query_part, keys_blocked[kblock], preferred_element_type=jnp.float32
            )
            * scale
        )
        same = query_images[:, None] == images_blocked[kblock][None, :]
        return jnp.where(same[None], scores, -1e30)

    def scan_stats(kblock, carry):
        row_max, row_sum = carry
        scores = block_scores(kblock)
        new_max = jnp.maximum(row_max, jnp.max(scores, axis=-1))
        row_sum = row_sum * jnp.exp(row_max - new_max) + jnp.sum(
            jnp.exp(scores - new_max[..., None]), axis=-1
        )
        return (new_max, row_sum)

    start_max = jnp.full((local_heads, q_block), -1e30, jnp.float32)
    start_sum = jnp.zeros((local_heads, q_block), jnp.float32)
    row_max, row_sum = lax.fori_loop(block_first, block_last, scan_stats, (start_max, start_sum))

    def add_values(kblock, totals):
        scores = block_scores(kblock)
        weights = (jnp.exp(scores - row_max[..., None]) / row_sum[..., None]).astype(jnp.bfloat16)
        return totals + jnp.einsum(
            "hqk,khd->qhd", weights, values_blocked[kblock], preferred_element_type=jnp.float32
        )

    totals = lax.fori_loop(
        block_first, block_last, add_values, jnp.zeros((q_block, local_heads, HDIM), jnp.float32)
    )
    return totals.reshape(q_block, local_heads * HDIM).astype(jnp.bfloat16)


def layer(tokens, segments, gain_attn, w_qkv, w_out, gain_mlp, w_up, w_down_t, gain_merge, w_proj):
    both = lax.all_gather(jnp.stack([w_up, w_down_t]), ("zx", "core", "tok"), axis=2, tiled=True)
    up_full, down_full = both[0], both[1]
    inputs = tokens.astype(jnp.float32)
    normed = layer_norm(inputs, gain_attn).astype(jnp.bfloat16)
    local_width = w_qkv.shape[2]
    joined = w_qkv.reshape(w_qkv.shape[0], 3 * local_width)
    stacked = jnp.dot(
        permute_gather(normed, "tok"),
        joined,
        preferred_element_type=jnp.float32,
    ).astype(jnp.bfloat16)
    group = stacked.shape[0]
    local_heads = local_width // HDIM
    q_block = min(512, group)
    k_block = min(128, group)
    scale = 1.0 / math.sqrt(HDIM)
    queries = stacked[:, :local_width]
    keys_blocked = stacked[:, local_width : 2 * local_width].reshape(
        group // k_block, k_block, local_heads, HDIM
    )
    values_blocked = stacked[:, 2 * local_width :].reshape(
        group // k_block, k_block, local_heads, HDIM
    )
    images = segments[0]
    images_blocked = images.reshape(group // k_block, k_block)
    outputs = []
    for block in range(group // q_block):
        outputs.append(
            attend_block(
                queries,
                keys_blocked,
                values_blocked,
                images,
                images_blocked,
                block * q_block,
                q_block,
                k_block,
                scale,
            )
        )
    heads_out = jnp.concatenate(outputs, axis=0)
    attended = permute_scatter(
        jnp.dot(heads_out, w_out, preferred_element_type=jnp.float32).astype(jnp.bfloat16),
        "tok",
    )
    first = (inputs + attended).astype(jnp.bfloat16)
    normed_mlp = layer_norm(first.astype(jnp.float32), gain_mlp).astype(jnp.bfloat16)
    mlp_out = hidden_fold(normed_mlp, (up_full, down_full))
    second = first.astype(jnp.float32) + mlp_out
    normed_merge = layer_norm(second, gain_merge).astype(jnp.bfloat16)
    merged = normed_merge.reshape(inputs.shape[0] // 4, 4 * inputs.shape[1])
    projected = jnp.dot(
        permute_gather(merged, "tok"),
        w_proj,
        preferred_element_type=jnp.float32,
    ).astype(jnp.bfloat16)
    return lax.all_to_all(projected, ("zx", "core"), split_axis=0, concat_axis=0, tiled=True)


def solution(mesh):
    devices = mesh.devices
    split = Mesh(devices.reshape(devices.shape[0] // 2, 2, devices.shape[1]), ("zx", "core", "tok"))
    rows = ("zx", "core")
    return jax.shard_map(
        layer,
        mesh=split,
        in_specs=(
            P(rows + ("tok",), None),
            P(rows, None),
            P(),
            P(None, None, "tok"),
            P("tok", None),
            P(),
            P(None, rows + ("tok",)),
            P(None, rows + ("tok",)),
            P(),
            P(None, "tok"),
        ),
        out_specs=P(rows, "tok"),
        check_vma=False,
    )
```

```python
import math

import jax
import jax.numpy as jnp
from jax import lax
from jax.sharding import Mesh, PartitionSpec as P


HDIM = 80


def layer_norm(values, gain):
    mean = jnp.mean(values, axis=-1, keepdims=True)
    centered = values - mean
    spread = jnp.mean(centered * centered, axis=-1, keepdims=True)
    return centered * lax.rsqrt(spread + 1e-06) * gain


def hidden_half(rows, pieces):
    hidden = jax.nn.gelu(
        lax.dot_general(
            rows, pieces[0], (((1,), (1,)), ((), ())), preferred_element_type=jnp.float32
        ),
        approximate=False,
    ).astype(jnp.bfloat16)
    return jnp.dot(hidden, pieces[1], preferred_element_type=jnp.float32)


def permute_gather(rows, axis):
    count = lax.axis_size(axis)
    here = lax.axis_index(axis)
    shifted = [rows] + [
        lax.ppermute(rows, axis, [(i, (i + s) % count) for i in range(count)])
        for s in range(1, count)
    ]
    stacked = jnp.stack(shifted)
    blocks = [
        lax.dynamic_index_in_dim(stacked, (here - source) % count, axis=0, keepdims=False)
        for source in range(count)
    ]
    return jnp.concatenate(blocks, axis=0)


def permute_scatter(parts, axis):
    count = lax.axis_size(axis)
    here = lax.axis_index(axis)
    blocks = parts.reshape(count, parts.shape[0] // count, parts.shape[1])
    total = lax.dynamic_index_in_dim(blocks, here, axis=0, keepdims=False).astype(jnp.float32)
    for s in range(1, count):
        outgoing = lax.dynamic_index_in_dim(blocks, (here + s) % count, axis=0, keepdims=False)
        incoming = lax.ppermute(outgoing, axis, [(i, (i + s) % count) for i in range(count)])
        total = total + incoming.astype(jnp.float32)
    return total


def attend_block(
    queries,
    keys_blocked,
    values_blocked,
    images,
    images_blocked,
    first_row,
    q_block,
    k_block,
    scale,
):
    local_heads = keys_blocked.shape[2]
    query_part = queries[first_row : first_row + q_block].reshape(q_block, local_heads, HDIM)
    query_images = images[first_row : first_row + q_block]
    key_first = jnp.sum((images < images[first_row]).astype(jnp.int32))
    key_last = jnp.sum((images <= images[first_row + q_block - 1]).astype(jnp.int32))
    block_first = key_first // k_block
    block_last = (key_last + k_block - 1) // k_block

    def block_scores(kblock):
        scores = (
            jnp.einsum(
                "qhd,khd->hqk", query_part, keys_blocked[kblock], preferred_element_type=jnp.float32
            )
            * scale
        )
        same = query_images[:, None] == images_blocked[kblock][None, :]
        return jnp.where(same[None], scores, -1e30)

    def scan_stats(kblock, carry):
        row_max, row_sum = carry
        scores = block_scores(kblock)
        new_max = jnp.maximum(row_max, jnp.max(scores, axis=-1))
        row_sum = row_sum * jnp.exp(row_max - new_max) + jnp.sum(
            jnp.exp(scores - new_max[..., None]), axis=-1
        )
        return (new_max, row_sum)

    start_max = jnp.full((local_heads, q_block), -1e30, jnp.float32)
    start_sum = jnp.zeros((local_heads, q_block), jnp.float32)
    row_max, row_sum = lax.fori_loop(block_first, block_last, scan_stats, (start_max, start_sum))

    def add_values(kblock, totals):
        scores = block_scores(kblock)
        weights = (jnp.exp(scores - row_max[..., None]) / row_sum[..., None]).astype(jnp.bfloat16)
        return totals + jnp.einsum(
            "hqk,khd->qhd", weights, values_blocked[kblock], preferred_element_type=jnp.float32
        )

    totals = lax.fori_loop(
        block_first, block_last, add_values, jnp.zeros((q_block, local_heads, HDIM), jnp.float32)
    )
    return totals.reshape(q_block, local_heads * HDIM).astype(jnp.bfloat16)


def layer(tokens, segments, gain_attn, w_qkv, w_out, gain_mlp, w_up, w_down_t, gain_merge, w_proj):
    own = lax.all_gather(jnp.stack([w_up.T, w_down_t.T]), ("zx", "tok"), axis=1, tiled=True)
    other = lax.ppermute(own, "core", [(0, 1), (1, 0)])
    inputs = tokens.astype(jnp.float32)
    normed = layer_norm(inputs, gain_attn).astype(jnp.bfloat16)
    local_width = w_qkv.shape[2]
    joined = w_qkv.reshape(w_qkv.shape[0], 3 * local_width)
    stacked = jnp.dot(
        permute_gather(normed, "tok"),
        joined,
        preferred_element_type=jnp.float32,
    ).astype(jnp.bfloat16)
    group = stacked.shape[0]
    local_heads = local_width // HDIM
    q_block = min(512, group)
    k_block = min(128, group)
    scale = 1.0 / math.sqrt(HDIM)
    queries = stacked[:, :local_width]
    keys_blocked = stacked[:, local_width : 2 * local_width].reshape(
        group // k_block, k_block, local_heads, HDIM
    )
    values_blocked = stacked[:, 2 * local_width :].reshape(
        group // k_block, k_block, local_heads, HDIM
    )
    images = segments[0]
    images_blocked = images.reshape(group // k_block, k_block)
    outputs = []
    for block in range(group // q_block):
        outputs.append(
            attend_block(
                queries,
                keys_blocked,
                values_blocked,
                images,
                images_blocked,
                block * q_block,
                q_block,
                k_block,
                scale,
            )
        )
    heads_out = jnp.concatenate(outputs, axis=0)
    attended = permute_scatter(
        jnp.dot(heads_out, w_out, preferred_element_type=jnp.float32).astype(jnp.bfloat16),
        "tok",
    )
    first = (inputs + attended).astype(jnp.bfloat16)
    normed_mlp = layer_norm(first.astype(jnp.float32), gain_mlp).astype(jnp.bfloat16)
    mlp_out = hidden_half(normed_mlp, own) + hidden_half(normed_mlp, other)
    second = first.astype(jnp.float32) + mlp_out
    normed_merge = layer_norm(second, gain_merge).astype(jnp.bfloat16)
    merged = normed_merge.reshape(inputs.shape[0] // 4, 4 * inputs.shape[1])
    projected = jnp.dot(
        permute_gather(merged, "tok"),
        w_proj,
        preferred_element_type=jnp.float32,
    ).astype(jnp.bfloat16)
    return lax.all_to_all(projected, ("zx", "core"), split_axis=0, concat_axis=0, tiled=True)


def solution(mesh):
    devices = mesh.devices
    split = Mesh(devices.reshape(devices.shape[0] // 2, 2, devices.shape[1]), ("zx", "core", "tok"))
    rows = ("zx", "core")
    return jax.shard_map(
        layer,
        mesh=split,
        in_specs=(
            P(rows + ("tok",), None),
            P(rows, None),
            P(),
            P(None, None, "tok"),
            P("tok", None),
            P(),
            P(None, rows + ("tok",)),
            P(None, rows + ("tok",)),
            P(),
            P(None, "tok"),
        ),
        out_specs=P(rows, "tok"),
        check_vma=False,
    )
```
